128 devices in a mesh: blk: 16 (over z_hi, y, core), freq: 8 (over z_lo, x).
Axes of the slice: x: 4, y: 4, z: 4 (z_hi: 2, z_lo: 2; z = z_hi * 2 + z_lo), core: 2. Of those that a mesh axis runs over, the one named last changes fastest.
Arguments:
- raw_voltages: bfloat16 [512, 530432], P(('blk', 'freq')), may hold values from -6 to 6
- filter_taps: float32 [4, 2048], replicated, may hold values from -3 to 3
- input_order: int32 [512], P('blk'), may hold values from 0 to 511, as said below
- chan_order: int32 [1024], replicated, may hold values from 0 to 1023, each once
Outputs:
- visibilities: float32 [2, 9, 32, 512, 1024], P(None, None, None, 'blk', 'freq')
The draws below stay inside these ranges and needn't reach their ends.
Inputs may be any that keep to these rules, and one draw needn't show every extreme that they name: input_order is a permutation, and slot k holds a raw input of the same aligned block of 32 slots as k. `chan_order`: each channel once.
All inputs are finite; a program needn't handle non-finite values.
Results may differ from the reference program's by a relative error of at most 0.0029.
Values may be sent and summed in bfloat16 or wider, within the bound.
No kernel may reach another device: no remote copies, remote signals or barrier semaphores. Data moves between devices by JAX's collectives and lax.ppermute only.
A program may use at most 128 MiB of HBM per device.

```python
import math
import jax
import jax.numpy as jnp
from jax import lax

INPUTS = 512
CH = 1024
TAPS = 4
SPECTRA = 256
SAMPLES = 530432
TILE = 32
STEPS = 9


def draw_input_order(key, part):
    tile_count = INPUTS // TILE
    scores = jax.random.randint(key, (tile_count, TILE), 0, 1 << 20) * TILE + jnp.arange(TILE, dtype=jnp.int32)[None, :]
    within = jnp.argsort(scores, axis=1, stable=True).astype(jnp.int32)
    starts = (jnp.arange(tile_count, dtype=jnp.int32) * TILE)[:, None]
    return (within + starts).reshape(INPUTS).astype(jnp.int32)


def levels(stream_key, dims, pieces, least, high):
    factor_of = 1.0
    for dim, shards_of in pieces:
        draws = jax.random.uniform(jax.random.fold_in(jax.random.fold_in(stream_key, 6), dim), (shards_of,), jnp.float32, least / len(pieces), high / len(pieces))
        factor_of = factor_of * jnp.repeat(jnp.exp(draws), dims[dim] // shards_of).reshape((-1,) + (1,) * (len(dims) - 1 - dim))
    return factor_of


def noise(own_key, extent, spread, bound, cuts=(), held_as=jnp.bfloat16):
    entries = spread * jax.random.normal(own_key, extent, jnp.float32)
    if cuts:
        entries = entries * levels(own_key, extent, cuts, -0.22, 0.18)
    return jnp.clip(entries, -bound, bound).astype(held_as)


def setup_inputs(seed: int = 0) -> dict:
    seeds = jax.random.split(jax.random.key(seed), 5)
    return {
        "raw_voltages": noise(seeds[0], (INPUTS, SAMPLES), 1.0, 6.0, ((0, 128),)),
        "filter_taps": noise(seeds[1], (TAPS, 2 * CH), TAPS ** -0.5, 3.0, (), jnp.float32),
        "input_order": draw_input_order(jax.random.fold_in(seeds[4], 71), 0),
        "chan_order": jax.random.permutation(seeds[3], CH).astype(jnp.int32),
    }


def make_table(chan_order):
    channel_count = chan_order.shape[0]
    sample_index = jnp.arange(2 * channel_count, dtype=jnp.int32)
    product = sample_index[:, None] * chan_order[None, :] % (2 * channel_count)
    phase_arg = product.astype(jnp.float32) * (math.pi / channel_count)
    return jnp.concatenate([jnp.cos(phase_arg), -jnp.sin(phase_arg)], axis=1) / math.sqrt(channel_count)

def filter_bank(raw_voltages, filter_taps, dft_table):
    input_count = raw_voltages.shape[0]
    channel_count = dft_table.shape[1] // 2
    frames = raw_voltages.astype(jnp.float32).reshape(input_count, SPECTRA + TAPS - 1, 2 * channel_count)
    filtered = filter_taps[0] * frames[:, 0:SPECTRA]
    for tap_index in range(1, TAPS):
        filtered = filtered + filter_taps[tap_index] * frames[:, tap_index:tap_index + SPECTRA]
    transformed = jnp.dot(filtered.reshape(input_count * SPECTRA, 2 * channel_count), dft_table, precision=lax.Precision.HIGHEST)
    transformed = transformed.reshape(input_count, SPECTRA, 2, channel_count).transpose(0, 2, 1, 3)
    return transformed.astype(jnp.bfloat16)

def reference(raw_voltages, filter_taps, input_order, chan_order):
    dft_table = make_table(chan_order)
    tile_count = INPUTS // TILE
    blocks = raw_voltages.reshape(tile_count, TILE, SAMPLES)
    spectra = lax.map(lambda block: filter_bank(block, filter_taps, dft_table), blocks)
    spectra = spectra.reshape(INPUTS, 2, SPECTRA, CH)
    slotted = spectra[input_order.astype(jnp.int32)]
    tile_blocks = slotted.reshape(tile_count, TILE, 2, SPECTRA, CH)
    plain = tile_blocks.reshape(tile_count, TILE, 2 * SPECTRA, CH).astype(jnp.float32)
    rotated = jnp.concatenate([tile_blocks[:, :, 1], -tile_blocks[:, :, 0]], axis=2).astype(jnp.float32)
    results = []
    for offset in range(STEPS):
        partners = jnp.roll(plain, offset, axis=0)
        vis_real = jnp.einsum('bjtc,bitc->jbic', partners, plain) / SPECTRA
        vis_imag = jnp.einsum('bjtc,bitc->jbic', partners, rotated) / SPECTRA
        results.append(jnp.stack([vis_real.reshape(TILE, INPUTS, CH), vis_imag.reshape(TILE, INPUTS, CH)]))
    return jnp.stack(results, axis=1)
```

```python
import math

import numpy as np
import jax
import jax.numpy as jnp
from jax import lax
from jax.sharding import PartitionSpec as P

TAPS = 4
SPECTRA = 256


def phase_table(chans, rows, period):
    sample_index = jnp.arange(rows, dtype=jnp.int32)
    product = sample_index[:, None] * chans[None, :] % period
    phase_arg = product.astype(jnp.float32) * (math.pi / (period // 2))
    return jnp.cos(phase_arg), jnp.sin(phase_arg)


def make_table(chans):
    channel_count = chans.shape[0]
    period = 2 * channel_count
    inner_rows = 64
    outer_rows = period // inner_rows
    inner_cos, inner_sin = phase_table(chans, inner_rows, period)
    outer_chans = chans * inner_rows % period
    outer_cos, outer_sin = phase_table(outer_chans, outer_rows, period)
    cos = outer_cos[:, None, :] * inner_cos[None] - outer_sin[:, None, :] * inner_sin[None]
    sin = outer_sin[:, None, :] * inner_cos[None] + outer_cos[:, None, :] * inner_sin[None]
    scale = 1.0 / math.sqrt(channel_count)
    table = jnp.stack([cos * scale, -sin * scale], axis=-1)
    return table.reshape(period, 2 * channel_count)


def per_device(raw_voltages, filter_taps, input_order, chan_order):
    n_blk = lax.axis_size("blk")
    n_freq = lax.axis_size("freq")
    n_dev = n_blk * n_freq
    channel_count = chan_order.shape[0]
    width = channel_count // n_freq
    chunk = width // n_blk
    steps = n_blk // 2 + 1
    tile = input_order.shape[0]
    local_inputs = raw_voltages.shape[0]
    frame = 2 * channel_count

    dest_b = np.arange(n_blk)[:, None, None]
    dest_f = np.arange(n_freq)[None, :, None]
    within = np.arange(chunk)[None, None, :]
    position = (dest_f * width + dest_b * chunk + within).reshape(-1)
    table = make_table(chan_order[position])

    frames = raw_voltages.astype(jnp.float32).reshape(local_inputs, SPECTRA + TAPS - 1, frame)
    filtered = filter_taps[0] * frames[:, 0:SPECTRA]
    for tap_index in range(1, TAPS):
        filtered = filtered + filter_taps[tap_index] * frames[:, tap_index : tap_index + SPECTRA]
    spectra = jnp.dot(
        filtered.reshape(local_inputs * SPECTRA, frame),
        table,
        precision=lax.Precision.HIGHEST,
    ).astype(jnp.bfloat16)
    spectra = spectra.reshape(local_inputs, SPECTRA, n_dev, chunk, 2).transpose(2, 3, 0, 4, 1)

    gathered = lax.all_to_all(spectra, ("blk", "freq"), 0, 0, tiled=True)
    total_inputs = n_dev * local_inputs
    gathered = gathered.transpose(1, 0, 2, 3, 4).reshape(chunk, total_inputs, 2, SPECTRA)

    slot_order = lax.all_gather(input_order, "blk", tiled=True)
    slotted = jnp.take(gathered, slot_order, axis=1)
    plain = slotted.reshape(chunk, total_inputs, 2 * SPECTRA)
    rotated = jnp.concatenate([slotted[:, :, 1], -slotted[:, :, 0]], axis=2)

    scale = 1.0 / SPECTRA
    doubled = jnp.concatenate([plain, plain], axis=1)
    rows = steps * tile
    blocks = []
    for own in range(n_blk):
        start = (own - steps + 1) % n_blk * tile
        partners = doubled[:, start : start + rows]
        mine = jnp.concatenate(
            [plain[:, own * tile : (own + 1) * tile], rotated[:, own * tile : (own + 1) * tile]],
            axis=1,
        )
        blocks.append(
            jnp.einsum("kpt,kit->kpi", partners, mine, preferred_element_type=jnp.float32)
        )
    banded = jnp.stack(blocks).reshape(n_blk, chunk, steps, tile, 2, tile)[:, :, ::-1]
    banded = banded.transpose(0, 4, 2, 3, 1, 5).reshape(n_blk, 2, steps, tile, chunk * tile) * scale

    returned = lax.all_to_all(banded, "blk", 0, 0, tiled=True)
    returned = returned.reshape(n_blk, 2, steps, tile, chunk, tile)
    return returned.transpose(1, 2, 3, 5, 0, 4).reshape(2, steps, tile, tile, n_blk * chunk)


def solution(mesh):
    placed = (P(("blk", "freq"), None), P(), P("blk"), P())
    return jax.shard_map(
        per_device,
        mesh=mesh,
        in_specs=placed,
        out_specs=P(None, None, None, "blk", "freq"),
        check_vma=False,
    )
```

```python
import math

import numpy as np
import jax
import jax.numpy as jnp
from jax import lax
from jax.sharding import PartitionSpec as P

TAPS = 4
SPECTRA = 256


def phase_table(chans, rows, period):
    sample_index = jnp.arange(rows, dtype=jnp.int32)
    product = sample_index[:, None] * chans[None, :] % period
    phase_arg = product.astype(jnp.float32) * (math.pi / (period // 2))
    return jnp.cos(phase_arg), jnp.sin(phase_arg)


def make_table(chans):
    channel_count = chans.shape[0]
    period = 2 * channel_count
    inner_rows = 64
    outer_rows = period // inner_rows
    inner_cos, inner_sin = phase_table(chans, inner_rows, period)
    outer_chans = chans * inner_rows % period
    outer_cos, outer_sin = phase_table(outer_chans, outer_rows, period)
    scale = 1.0 / math.sqrt(channel_count)
    cos = outer_cos[:, None, :] * inner_cos[None] - outer_sin[:, None, :] * inner_sin[None]
    sin = outer_sin[:, None, :] * inner_cos[None] + outer_cos[:, None, :] * inner_sin[None]
    return (cos * scale).reshape(period, channel_count), (sin * -scale).reshape(period, channel_count)


def per_device(raw_voltages, filter_taps, input_order, chan_order):
    n_blk = lax.axis_size("blk")
    n_freq = lax.axis_size("freq")
    n_dev = n_blk * n_freq
    channel_count = chan_order.shape[0]
    width = channel_count // n_freq
    chunk = width // n_blk
    steps = n_blk // 2 + 1
    tile = input_order.shape[0]
    local_inputs = raw_voltages.shape[0]
    frame = 2 * channel_count

    slot_order = lax.all_gather(input_order.astype(jnp.float32), "blk", tiled=True)

    dest_b = np.arange(n_blk)[:, None, None]
    dest_f = np.arange(n_freq)[None, :, None]
    within = np.arange(chunk)[None, None, :]
    position = (dest_f * width + dest_b * chunk + within).reshape(-1)
    cos_table, sin_table = make_table(chan_order[position])

    frames = raw_voltages.astype(jnp.float32).reshape(local_inputs, SPECTRA + TAPS - 1, frame)
    filtered = filter_taps[0] * frames[:, 0:SPECTRA]
    for tap_index in range(1, TAPS):
        filtered = filtered + filter_taps[tap_index] * frames[:, tap_index : tap_index + SPECTRA]
    filtered = filtered.reshape(local_inputs * SPECTRA, frame)
    parts = [
        jnp.einsum("mc,nm->cn", part, filtered, precision=lax.Precision.HIGH)
        for part in (cos_table, sin_table)
    ]
    spectra = jnp.stack(parts, axis=1).astype(jnp.bfloat16)
    spectra = spectra.reshape(n_dev, chunk, 2, local_inputs, SPECTRA).transpose(0, 1, 3, 2, 4)

    gathered = lax.all_to_all(spectra, ("blk", "freq"), 0, 0, tiled=True)
    total_inputs = n_dev * local_inputs
    gathered = gathered.transpose(1, 0, 2, 3, 4).reshape(chunk, total_inputs, 2, SPECTRA)

    slotted = jnp.take(gathered, slot_order.astype(jnp.int32), axis=1)
    plain = slotted.reshape(chunk, total_inputs, 2 * SPECTRA)
    rotated = jnp.concatenate([slotted[:, :, 1], -slotted[:, :, 0]], axis=2)
    both = jnp.concatenate([plain, rotated], axis=1)

    gram = jnp.einsum("kat,kpt->kap", both, plain, preferred_element_type=jnp.float32)
    gram = gram.reshape(chunk, 2, n_blk, tile, total_inputs)
    doubled = jnp.concatenate([gram, gram], axis=-1)
    rows = steps * tile
    blocks = []
    for own in range(n_blk):
        start = (own - steps + 1) % n_blk * tile
        blocks.append(doubled[:, :, own, :, start : start + rows])
    banded = jnp.stack(blocks).transpose(0, 2, 1, 3, 4) * (1.0 / SPECTRA)

    returned = lax.all_to_all(banded, "blk", 0, 0, tiled=True)
    returned = returned.reshape(n_blk, 2, chunk, tile, steps, tile)[:, :, :, :, ::-1]
    return returned.transpose(1, 4, 5, 3, 0, 2).reshape(2, steps, tile, tile, n_blk * chunk)


def solution(mesh):
    placed = (P(("blk", "freq"), None), P(), P("blk"), P())
    return jax.shard_map(
        per_device,
        mesh=mesh,
        in_specs=placed,
        out_specs=P(None, None, None, "blk", "freq"),
        check_vma=False,
    )
```

```python
import math

import numpy as np
import jax
import jax.numpy as jnp
from jax import lax
from jax.sharding import PartitionSpec as P

TAPS = 4
SPECTRA = 256


def phase_table(chans, rows, period):
    sample_index = jnp.arange(rows, dtype=jnp.int32)
    product = sample_index[:, None] * chans[None, :] % period
    phase_arg = product.astype(jnp.float32) * (math.pi / (period // 2))
    return jnp.cos(phase_arg), jnp.sin(phase_arg)


def make_table(chans):
    channel_count = chans.shape[0]
    period = 2 * channel_count
    inner_rows = 64
    outer_rows = period // inner_rows
    inner_cos, inner_sin = phase_table(chans, inner_rows, period)
    outer_chans = chans * inner_rows % period
    outer_cos, outer_sin = phase_table(outer_chans, outer_rows, period)
    scale = 1.0 / math.sqrt(channel_count)
    cos = outer_cos[:, None, :] * inner_cos[None] - outer_sin[:, None, :] * inner_sin[None]
    sin = outer_sin[:, None, :] * inner_cos[None] + outer_cos[:, None, :] * inner_sin[None]
    return (cos * scale).reshape(period, channel_count), (sin * -scale).reshape(period, channel_count)


def per_device(raw_voltages, filter_taps, input_order, chan_order):
    n_blk = lax.axis_size("blk")
    n_freq = lax.axis_size("freq")
    n_dev = n_blk * n_freq
    channel_count = chan_order.shape[0]
    width = channel_count // n_freq
    chunk = width // n_blk
    steps = n_blk // 2 + 1
    tile = input_order.shape[0]
    local_inputs = raw_voltages.shape[0]
    frame = 2 * channel_count

    slot_order = lax.all_gather(input_order.astype(jnp.float32), "blk", tiled=True)
    slot_order, chan_order = lax.optimization_barrier((slot_order, chan_order))

    dest_b = np.arange(n_blk)[:, None, None]
    dest_f = np.arange(n_freq)[None, :, None]
    within = np.arange(chunk)[None, None, :]
    position = (dest_f * width + dest_b * chunk + within).reshape(-1)
    cos_table, sin_table = make_table(chan_order[position])

    frames = raw_voltages.astype(jnp.float32).reshape(local_inputs, SPECTRA + TAPS - 1, frame)
    filtered = filter_taps[0] * frames[:, 0:SPECTRA]
    for tap_index in range(1, TAPS):
        filtered = filtered + filter_taps[tap_index] * frames[:, tap_index : tap_index + SPECTRA]
    filtered = filtered.reshape(local_inputs * SPECTRA, frame)
    parts = [
        jnp.einsum("mc,nm->cn", part, filtered, precision=lax.Precision.HIGH)
        for part in (cos_table, sin_table)
    ]
    spectra = jnp.stack(parts, axis=1).astype(jnp.bfloat16)
    spectra = spectra.reshape(n_dev, chunk, 2, local_inputs, SPECTRA).transpose(0, 1, 3, 2, 4)

    gathered = lax.all_to_all(spectra, ("blk", "freq"), 0, 0, tiled=True)
    total_inputs = n_dev * local_inputs
    gathered = gathered.transpose(1, 0, 2, 3, 4).reshape(chunk, total_inputs, 2, SPECTRA)

    slotted = jnp.take(gathered, slot_order.astype(jnp.int32), axis=1)
    plain = slotted.reshape(chunk, total_inputs, 2 * SPECTRA)
    rotated = jnp.concatenate([slotted[:, :, 1], -slotted[:, :, 0]], axis=2)
    both = jnp.concatenate([plain, rotated], axis=1)

    gram = jnp.einsum("kat,kpt->kap", both, plain, preferred_element_type=jnp.float32)
    gram = gram.reshape(chunk, 2, n_blk, tile, total_inputs)
    doubled = jnp.concatenate([gram, gram], axis=-1)
    rows = steps * tile
    blocks = []
    for own in range(n_blk):
        start = (own - steps + 1) % n_blk * tile
        blocks.append(doubled[:, :, own, :, start : start + rows])
    banded = jnp.stack(blocks).transpose(0, 2, 3, 1, 4) * (1.0 / SPECTRA)

    returned = lax.all_to_all(banded, "blk", 0, 0, tiled=True)
    returned = returned.transpose(1, 2, 0, 3, 4).reshape(2, tile, n_blk * chunk, steps, tile)
    returned = returned[:, :, :, ::-1].transpose(0, 1, 3, 4, 2)
    return returned.transpose(0, 2, 3, 1, 4)


def solution(mesh):
    placed = (P(("blk", "freq"), None), P(), P("blk"), P())
    return jax.shard_map(
        per_device,
        mesh=mesh,
        in_specs=placed,
        out_specs=P(None, None, None, "blk", "freq"),
        check_vma=False,
    )
```

```python
import math

import numpy as np
import jax
import jax.numpy as jnp
from jax import lax
from jax.sharding import PartitionSpec as P

TAPS = 4
SPECTRA = 256


def phase_table(chans, rows, period):
    sample_index = jnp.arange(rows, dtype=jnp.int32)
    product = sample_index[:, None] * chans[None, :] % period
    phase_arg = product.astype(jnp.float32) * (math.pi / (period // 2))
    return jnp.cos(phase_arg), jnp.sin(phase_arg)


def make_table(chans):
    channel_count = chans.shape[0]
    period = 2 * channel_count
    inner_rows = 64
    outer_rows = period // inner_rows
    inner_cos, inner_sin = phase_table(chans, inner_rows, period)
    outer_chans = chans * inner_rows % period
    outer_cos, outer_sin = phase_table(outer_chans, outer_rows, period)
    scale = 1.0 / math.sqrt(channel_count)
    cos = outer_cos[:, None, :] * inner_cos[None] - outer_sin[:, None, :] * inner_sin[None]
    sin = outer_sin[:, None, :] * inner_cos[None] + outer_cos[:, None, :] * inner_sin[None]
    return (cos * scale).reshape(period, channel_count), (sin * -scale).reshape(period, channel_count)


def per_device(raw_voltages, filter_taps, input_order, chan_order):
    n_blk = lax.axis_size("blk")
    n_freq = lax.axis_size("freq")
    n_dev = n_blk * n_freq
    channel_count = chan_order.shape[0]
    width = channel_count // n_freq
    chunk = width // n_blk
    steps = n_blk // 2 + 1
    tile = input_order.shape[0]
    local_inputs = raw_voltages.shape[0]
    frame = 2 * channel_count

    slot_order = lax.all_gather(input_order.astype(jnp.float32), "blk", tiled=True)
    slot_order, chan_order = lax.optimization_barrier((slot_order, chan_order))

    dest_b = np.arange(n_blk)[:, None, None]
    dest_f = np.arange(n_freq)[None, :, None]
    within = np.arange(chunk)[None, None, :]
    position = (dest_f * width + dest_b * chunk + within).reshape(-1)
    cos_table, sin_table = make_table(chan_order[position])

    frames = raw_voltages.astype(jnp.float32).reshape(local_inputs, SPECTRA + TAPS - 1, frame)
    filtered = filter_taps[0] * frames[:, 0:SPECTRA]
    for tap_index in range(1, TAPS):
        filtered = filtered + filter_taps[tap_index] * frames[:, tap_index : tap_index + SPECTRA]
    filtered = filtered.reshape(local_inputs * SPECTRA, frame)
    parts = [
        jnp.einsum("mc,nm->cn", part, filtered, precision=lax.Precision.HIGH)
        for part in (cos_table, sin_table)
    ]
    spectra = jnp.stack(parts, axis=1).astype(jnp.bfloat16)
    spectra = spectra.reshape(n_dev, chunk, 2, local_inputs, SPECTRA).transpose(0, 1, 3, 2, 4)

    gathered = lax.all_to_all(spectra, ("blk", "freq"), 0, 0, tiled=True)
    total_inputs = n_dev * local_inputs
    gathered = gathered.transpose(1, 0, 2, 3, 4).reshape(chunk, total_inputs, 2, SPECTRA)

    slotted = jnp.take(gathered, slot_order.astype(jnp.int32), axis=1)
    plain = slotted.reshape(chunk, total_inputs, 2 * SPECTRA)
    rotated = jnp.concatenate([slotted[:, :, 1], -slotted[:, :, 0]], axis=2)
    both = jnp.concatenate([plain, rotated], axis=1)

    gram = jnp.einsum("kat,kpt->kap", both, plain, preferred_element_type=jnp.float32)
    gram = gram.reshape(chunk, 2, n_blk, tile, total_inputs)
    doubled = jnp.concatenate([gram, gram], axis=-1)
    rows = steps * tile
    blocks = []
    for own in range(n_blk):
        start = (own - steps + 1) % n_blk * tile
        blocks.append(doubled[:, :, own, :, start : start + rows])
    banded = jnp.stack(blocks).transpose(0, 2, 3, 1, 4) * (1.0 / SPECTRA)

    returned = lax.all_to_all(banded, "blk", 0, 0, tiled=True)
    eye = jnp.eye(n_blk * chunk, dtype=jnp.float32).reshape(n_blk, chunk, n_blk * chunk)
    turned = jnp.einsum("brikq,bkc->riqc", returned, eye, precision=lax.Precision.HIGHEST)
    turned = turned.reshape(2, tile, steps, tile, n_blk * chunk)[:, :, ::-1]
    return turned.transpose(0, 2, 3, 1, 4)


def solution(mesh):
    placed = (P(("blk", "freq"), None), P(), P("blk"), P())
    return jax.shard_map(
        per_device,
        mesh=mesh,
        in_specs=placed,
        out_specs=P(None, None, None, "blk", "freq"),
        check_vma=False,
    )
```

```python
import math

import numpy as np
import jax
import jax.numpy as jnp
from jax import lax
from jax.sharding import PartitionSpec as P

TAPS = 4
SPECTRA = 256


def phase_table(chans, rows, period):
    sample_index = jnp.arange(rows, dtype=jnp.int32)
    product = sample_index[:, None] * chans[None, :] % period
    phase_arg = product.astype(jnp.float32) * (math.pi / (period // 2))
    return jnp.cos(phase_arg), jnp.sin(phase_arg)


def make_table(chans, channel_count):
    period = 2 * channel_count
    inner_rows = 64
    outer_rows = period // inner_rows
    inner_cos, inner_sin = phase_table(chans, inner_rows, period)
    outer_chans = chans * inner_rows % period
    outer_cos, outer_sin = phase_table(outer_chans, outer_rows, period)
    scale = 1.0 / math.sqrt(channel_count)
    cos = outer_cos[:, None, :] * inner_cos[None] - outer_sin[:, None, :] * inner_sin[None]
    sin = outer_sin[:, None, :] * inner_cos[None] + outer_cos[:, None, :] * inner_sin[None]
    columns = chans.shape[0]
    return (cos * scale).reshape(period, columns), (sin * -scale).reshape(period, columns)


def per_device(raw_voltages, filter_taps, input_order, chan_order):
    n_blk = lax.axis_size("blk")
    n_freq = lax.axis_size("freq")
    n_dev = n_blk * n_freq
    channel_count = chan_order.shape[0]
    width = channel_count // n_freq
    chunk = width // n_blk
    halves = 2
    part_chunk = chunk // halves
    steps = n_blk // 2 + 1
    tile = input_order.shape[0]
    local_inputs = raw_voltages.shape[0]
    total_inputs = n_dev * local_inputs
    frame = 2 * channel_count
    rows = steps * tile

    slot_order = lax.all_gather(input_order.astype(jnp.float32), "blk", tiled=True)
    slot_order, chan_order = lax.optimization_barrier((slot_order, chan_order))
    slot_order = slot_order.astype(jnp.int32)

    frames = raw_voltages.astype(jnp.float32).reshape(local_inputs, SPECTRA + TAPS - 1, frame)
    filtered = filter_taps[0] * frames[:, 0:SPECTRA]
    for tap_index in range(1, TAPS):
        filtered = filtered + filter_taps[tap_index] * frames[:, tap_index : tap_index + SPECTRA]
    filtered = filtered.reshape(local_inputs * SPECTRA, frame)

    dest_b = np.arange(n_blk)[:, None, None]
    dest_f = np.arange(n_freq)[None, :, None]

    def half_spectra(half):
        within = np.arange(half * part_chunk, (half + 1) * part_chunk)[None, None, :]
        position = (dest_f * width + dest_b * chunk + within).reshape(-1)
        cos_table, sin_table = make_table(chan_order[position], channel_count)
        parts = [
            jnp.einsum("mc,nm->cn", part, filtered, precision=lax.Precision.HIGH)
            for part in (cos_table, sin_table)
        ]
        spectra = jnp.stack(parts, axis=1).astype(jnp.bfloat16)
        spectra = spectra.reshape(n_dev, part_chunk, 2, local_inputs, SPECTRA)
        return spectra.transpose(0, 1, 3, 2, 4)

    def half_band(spectra):
        gathered = lax.all_to_all(spectra, ("blk", "freq"), 0, 0, tiled=True)
        gathered = gathered.transpose(1, 0, 2, 3, 4).reshape(part_chunk, total_inputs, 2, SPECTRA)
        slotted = jnp.take(gathered, slot_order, axis=1)
        plain = slotted.reshape(part_chunk, total_inputs, 2 * SPECTRA)
        rotated = jnp.concatenate([slotted[:, :, 1], -slotted[:, :, 0]], axis=2)
        both = jnp.concatenate([plain, rotated], axis=1)
        gram = jnp.einsum("kat,kpt->kap", both, plain, preferred_element_type=jnp.float32)
        gram = gram.reshape(part_chunk, 2, n_blk, tile, total_inputs)
        doubled = jnp.concatenate([gram, gram], axis=-1)
        blocks = []
        for own in range(n_blk):
            start = (own - steps + 1) % n_blk * tile
            blocks.append(doubled[:, :, own, :, start : start + rows])
        return jnp.stack(blocks) * (1.0 / SPECTRA)

    def half_output(banded, half):
        returned = lax.all_to_all(banded, "blk", 0, 0, tiled=True)
        returned = returned.reshape(n_blk * part_chunk, 2 * tile * rows)
        source = np.arange(n_blk)[:, None] * chunk + half * part_chunk + np.arange(part_chunk)[None, :]
        select = (source.reshape(-1, 1) == np.arange(n_blk * chunk)[None, :]).astype(np.float32)
        return jnp.einsum("ax,ac->xc", returned, jnp.asarray(select), precision=lax.Precision.HIGHEST)

    spectra_parts = [half_spectra(half) for half in range(halves)]
    band_parts = [half_band(spectra) for spectra in spectra_parts]
    turned = half_output(band_parts[0], 0)
    for half in range(1, halves):
        turned = turned + half_output(band_parts[half], half)
    turned = turned.reshape(2, tile, steps, tile, n_blk * chunk)[:, :, ::-1]
    return turned.transpose(0, 2, 3, 1, 4)


def solution(mesh):
    placed = (P(("blk", "freq"), None), P(), P("blk"), P())
    return jax.shard_map(
        per_device,
        mesh=mesh,
        in_specs=placed,
        out_specs=P(None, None, None, "blk", "freq"),
        check_vma=False,
    )
```

```python
import math

import numpy as np
import jax
import jax.numpy as jnp
from jax import lax
from jax.sharding import PartitionSpec as P

TAPS = 4
SPECTRA = 256


def phase_table(chans, rows, period):
    sample_index = jnp.arange(rows, dtype=jnp.int32)
    product = sample_index[:, None] * chans[None, :] % period
    phase_arg = product.astype(jnp.float32) * (math.pi / (period // 2))
    return jnp.cos(phase_arg), jnp.sin(phase_arg)


def make_table(chans, channel_count):
    period = 2 * channel_count
    inner_rows = 64
    outer_rows = period // inner_rows
    inner_cos, inner_sin = phase_table(chans, inner_rows, period)
    outer_chans = chans * inner_rows % period
    outer_cos, outer_sin = phase_table(outer_chans, outer_rows, period)
    scale = 1.0 / math.sqrt(channel_count)
    cos = outer_cos[:, None, :] * inner_cos[None] - outer_sin[:, None, :] * inner_sin[None]
    sin = outer_sin[:, None, :] * inner_cos[None] + outer_cos[:, None, :] * inner_sin[None]
    columns = chans.shape[0]
    return (cos * scale).reshape(period, columns), (sin * -scale).reshape(period, columns)


def per_device(raw_voltages, filter_taps, input_order, chan_order):
    n_blk = lax.axis_size("blk")
    n_freq = lax.axis_size("freq")
    n_dev = n_blk * n_freq
    channel_count = chan_order.shape[0]
    width = channel_count // n_freq
    chunk = width // n_blk
    halves = 2
    part_chunk = chunk // halves
    steps = n_blk // 2 + 1
    tile = input_order.shape[0]
    local_inputs = raw_voltages.shape[0]
    total_inputs = n_dev * local_inputs
    frame = 2 * channel_count
    rows = steps * tile

    slot_order = lax.all_gather(input_order.astype(jnp.float32), "blk", tiled=True)
    slot_order, chan_order = lax.optimization_barrier((slot_order, chan_order))
    slot_order = slot_order.astype(jnp.int32)

    frames = raw_voltages.astype(jnp.float32).reshape(local_inputs, SPECTRA + TAPS - 1, frame)
    filtered = filter_taps[0] * frames[:, 0:SPECTRA]
    for tap_index in range(1, TAPS):
        filtered = filtered + filter_taps[tap_index] * frames[:, tap_index : tap_index + SPECTRA]
    filtered = filtered.reshape(local_inputs * SPECTRA, frame)

    dest_b = np.arange(n_blk)[:, None, None]
    dest_f = np.arange(n_freq)[None, :, None]

    def half_spectra(half):
        within = np.arange(half * part_chunk, (half + 1) * part_chunk)[None, None, :]
        position = (dest_f * width + dest_b * chunk + within).reshape(-1)
        cos_table, sin_table = make_table(chan_order[position], channel_count)
        parts = [
            jnp.einsum("mc,nm->cn", part, filtered, precision=lax.Precision.HIGH)
            for part in (cos_table, sin_table)
        ]
        spectra = jnp.stack(parts, axis=1).astype(jnp.bfloat16)
        spectra = spectra.reshape(n_dev, part_chunk, 2, local_inputs, SPECTRA)
        return spectra.transpose(0, 1, 3, 2, 4)

    def half_band(spectra):
        gathered = lax.all_to_all(spectra, ("blk", "freq"), 0, 0, tiled=True)
        gathered = gathered.transpose(1, 0, 2, 3, 4).reshape(part_chunk, total_inputs, 2, SPECTRA)
        slotted = jnp.take(gathered, slot_order, axis=1)
        plain = slotted.reshape(part_chunk, total_inputs, 2 * SPECTRA)
        rotated = jnp.concatenate([slotted[:, :, 1], -slotted[:, :, 0]], axis=2)
        both = jnp.concatenate([plain, rotated], axis=1)
        gram = jnp.einsum("kat,kpt->kap", both, plain, preferred_element_type=jnp.float32)
        gram = gram.reshape(part_chunk, 2, n_blk, tile, total_inputs)
        doubled = jnp.concatenate([gram, gram], axis=-1)
        blocks = []
        for own in range(n_blk):
            start = (own - steps + 1) % n_blk * tile
            blocks.append(doubled[:, :, own, :, start : start + rows])
        return (jnp.stack(blocks) * (1.0 / SPECTRA)).reshape(n_blk, -1)

    def half_output(banded, half):
        returned = lax.all_to_all(banded, "blk", 0, 0, tiled=True)
        returned = returned.reshape(n_blk, part_chunk, 2 * tile * rows)
        source = np.arange(n_blk)[:, None] * chunk + half * part_chunk + np.arange(part_chunk)[None, :]
        select = (source[:, :, None] == np.arange(n_blk * chunk)[None, None, :]).astype(np.float32)
        return jnp.einsum("bkx,bkc->xc", returned, jnp.asarray(select), precision=lax.Precision.HIGHEST)

    spectra_parts = [half_spectra(half) for half in range(halves)]
    band_parts = [half_band(spectra) for spectra in spectra_parts]
    turned = half_output(band_parts[0], 0)
    for half in range(1, halves):
        turned = turned + half_output(band_parts[half], half)
    turned = turned.reshape(2, tile, steps, tile, n_blk * chunk)[:, :, ::-1]
    return turned.transpose(0, 2, 3, 1, 4)


def solution(mesh):
    placed = (P(("blk", "freq"), None), P(), P("blk"), P())
    return jax.shard_map(
        per_device,
        mesh=mesh,
        in_specs=placed,
        out_specs=P(None, None, None, "blk", "freq"),
        check_vma=False,
    )
```

```python
import math

import numpy as np
import jax
import jax.numpy as jnp
from jax import lax
from jax.sharding import PartitionSpec as P

TAPS = 4
SPECTRA = 256


def phase_table(chans, rows, period):
    sample_index = jnp.arange(rows, dtype=jnp.int32)
    product = sample_index[:, None] * chans[None, :] % period
    phase_arg = product.astype(jnp.float32) * (math.pi / (period // 2))
    return jnp.cos(phase_arg), jnp.sin(phase_arg)


def make_table(chans, channel_count):
    period = 2 * channel_count
    inner_rows = 64
    outer_rows = period // inner_rows
    inner_cos, inner_sin = phase_table(chans, inner_rows, period)
    outer_chans = chans * inner_rows % period
    outer_cos, outer_sin = phase_table(outer_chans, outer_rows, period)
    scale = 1.0 / math.sqrt(channel_count)
    cos = outer_cos[:, None, :] * inner_cos[None] - outer_sin[:, None, :] * inner_sin[None]
    sin = outer_sin[:, None, :] * inner_cos[None] + outer_cos[:, None, :] * inner_sin[None]
    columns = chans.shape[0]
    return (cos * scale).reshape(period, columns), (sin * -scale).reshape(period, columns)


def per_device(raw_voltages, filter_taps, input_order, chan_order):
    n_blk = lax.axis_size("blk")
    n_freq = lax.axis_size("freq")
    n_dev = n_blk * n_freq
    channel_count = chan_order.shape[0]
    width = channel_count // n_freq
    chunk = width // n_blk
    halves = 4
    part_chunk = chunk // halves
    steps = n_blk // 2 + 1
    tile = input_order.shape[0]
    local_inputs = raw_voltages.shape[0]
    total_inputs = n_dev * local_inputs
    frame = 2 * channel_count
    rows = steps * tile

    spread = jnp.broadcast_to(input_order.astype(jnp.float32)[None], (n_dev, tile))
    slot_order = lax.all_to_all(spread, ("blk", "freq"), 0, 0, tiled=True)
    slot_order = slot_order.reshape(n_blk, n_freq, tile)[:, 0].reshape(-1).astype(jnp.int32)

    frames = raw_voltages.astype(jnp.float32).reshape(local_inputs, SPECTRA + TAPS - 1, frame)
    filtered = filter_taps[0] * frames[:, 0:SPECTRA]
    for tap_index in range(1, TAPS):
        filtered = filtered + filter_taps[tap_index] * frames[:, tap_index : tap_index + SPECTRA]
    filtered = filtered.reshape(local_inputs * SPECTRA, frame)

    dest_b = np.arange(n_blk)[:, None, None]
    dest_f = np.arange(n_freq)[None, :, None]

    def half_spectra(half):
        within = np.arange(half * part_chunk, (half + 1) * part_chunk)[None, None, :]
        position = (dest_f * width + dest_b * chunk + within).reshape(-1)
        cos_table, sin_table = make_table(chan_order[position], channel_count)
        parts = [
            jnp.einsum("mc,nm->cn", part, filtered, precision=lax.Precision.HIGH)
            for part in (cos_table, sin_table)
        ]
        spectra = jnp.stack(parts, axis=1).astype(jnp.bfloat16)
        spectra = spectra.reshape(n_dev, part_chunk, 2, local_inputs, SPECTRA)
        return spectra.transpose(0, 1, 3, 2, 4)

    def half_band(spectra):
        gathered = lax.all_to_all(spectra, ("blk", "freq"), 0, 0, tiled=True)
        gathered = gathered.transpose(1, 0, 2, 3, 4).reshape(part_chunk, total_inputs, 2, SPECTRA)
        slotted = jnp.take(gathered, slot_order, axis=1)
        plain = slotted.reshape(part_chunk, total_inputs, 2 * SPECTRA)
        rotated = jnp.concatenate([slotted[:, :, 1], -slotted[:, :, 0]], axis=2)
        both = jnp.concatenate([plain, rotated], axis=1)
        gram = jnp.einsum("kat,kpt->kap", both, plain, preferred_element_type=jnp.float32)
        gram = gram.reshape(part_chunk, 2, n_blk, tile, total_inputs)
        doubled = jnp.concatenate([gram, gram], axis=-1)
        blocks = []
        for own in range(n_blk):
            start = (own - steps + 1) % n_blk * tile
            blocks.append(doubled[:, :, own, :, start : start + rows])
        return jnp.stack(blocks) * (1.0 / SPECTRA)

    def half_output(banded, half):
        returned = lax.all_to_all(banded, "blk", 0, 0, tiled=True)
        returned = returned.reshape(n_blk * part_chunk, 2 * tile * rows)
        source = np.arange(n_blk)[:, None] * chunk + half * part_chunk + np.arange(part_chunk)[None, :]
        select = (source.reshape(-1, 1) == np.arange(n_blk * chunk)[None, :]).astype(np.float32)
        return jnp.einsum("ax,ac->xc", returned, jnp.asarray(select), precision=lax.Precision.HIGHEST)

    spectra_parts = [half_spectra(half) for half in range(halves)]
    band_parts = [half_band(spectra) for spectra in spectra_parts]
    turned = half_output(band_parts[0], 0)
    for half in range(1, halves):
        turned = turned + half_output(band_parts[half], half)
    turned = turned.reshape(2, tile, steps, tile, n_blk * chunk)[:, :, ::-1]
    return turned.transpose(0, 2, 3, 1, 4)


def solution(mesh):
    placed = (P(("blk", "freq"), None), P(), P("blk"), P())
    return jax.shard_map(
        per_device,
        mesh=mesh,
        in_specs=placed,
        out_specs=P(None, None, None, "blk", "freq"),
        check_vma=False,
    )
```

```python
import math

import numpy as np
import jax
import jax.numpy as jnp
from jax import lax
from jax.sharding import PartitionSpec as P

TAPS = 4
SPECTRA = 256


def phase_table(chans, rows, period):
    sample_index = jnp.arange(rows, dtype=jnp.int32)
    product = sample_index[:, None] * chans[None, :] % period
    phase_arg = product.astype(jnp.float32) * (math.pi / (period // 2))
    return jnp.cos(phase_arg), jnp.sin(phase_arg)


def make_table(chans, channel_count):
    period = 2 * channel_count
    inner_rows = 64
    outer_rows = period // inner_rows
    inner_cos, inner_sin = phase_table(chans, inner_rows, period)
    outer_chans = chans * inner_rows % period
    outer_cos, outer_sin = phase_table(outer_chans, outer_rows, period)
    scale = 1.0 / math.sqrt(channel_count)
    cos = outer_cos[:, None, :] * inner_cos[None] - outer_sin[:, None, :] * inner_sin[None]
    sin = outer_sin[:, None, :] * inner_cos[None] + outer_cos[:, None, :] * inner_sin[None]
    columns = chans.shape[0]
    return (cos * scale).reshape(period, columns), (sin * -scale).reshape(period, columns)


def per_device(raw_voltages, filter_taps, input_order, chan_order):
    n_blk = lax.axis_size("blk")
    n_freq = lax.axis_size("freq")
    n_dev = n_blk * n_freq
    channel_count = chan_order.shape[0]
    width = channel_count // n_freq
    chunk = width // n_blk
    halves = 2
    part_chunk = chunk // halves
    steps = n_blk // 2 + 1
    tile = input_order.shape[0]
    local_inputs = raw_voltages.shape[0]
    total_inputs = n_dev * local_inputs
    frame = 2 * channel_count
    rows = steps * tile

    spread = jnp.broadcast_to(input_order.astype(jnp.float32)[None], (n_dev, tile))
    slot_order = lax.all_to_all(spread, ("blk", "freq"), 0, 0, tiled=True)
    slot_order = slot_order.reshape(n_blk, n_freq, tile)[:, 0].reshape(-1).astype(jnp.int32)

    frames = raw_voltages.astype(jnp.float32).reshape(local_inputs, SPECTRA + TAPS - 1, frame)
    filtered = filter_taps[0] * frames[:, 0:SPECTRA]
    for tap_index in range(1, TAPS):
        filtered = filtered + filter_taps[tap_index] * frames[:, tap_index : tap_index + SPECTRA]
    filtered = filtered.reshape(local_inputs * SPECTRA, frame)

    dest_b = np.arange(n_blk)[:, None, None]
    dest_f = np.arange(n_freq)[None, :, None]

    def half_spectra(half):
        within = np.arange(half * part_chunk, (half + 1) * part_chunk)[None, None, :]
        position = (dest_f * width + dest_b * chunk + within).reshape(-1)
        cos_table, sin_table = make_table(chan_order[position], channel_count)
        parts = [
            jnp.einsum("mc,nm->cn", part, filtered, precision=lax.Precision.HIGH)
            for part in (cos_table, sin_table)
        ]
        spectra = jnp.stack(parts, axis=1).astype(jnp.bfloat16)
        spectra = spectra.reshape(n_dev, part_chunk, 2, local_inputs, SPECTRA)
        return spectra.transpose(0, 1, 3, 2, 4)

    def half_band(spectra):
        gathered = lax.all_to_all(spectra, ("blk", "freq"), 0, 0, tiled=True)
        gathered = gathered.transpose(1, 0, 2, 3, 4).reshape(part_chunk, total_inputs, 2, SPECTRA)
        slotted = jnp.take(gathered, slot_order, axis=1)
        plain = slotted.reshape(part_chunk, total_inputs, 2 * SPECTRA)
        rotated = jnp.concatenate([slotted[:, :, 1], -slotted[:, :, 0]], axis=2)
        both = jnp.concatenate([plain, rotated], axis=1)
        gram = jnp.einsum("kat,kpt->kap", both, plain, preferred_element_type=jnp.float32)
        gram = gram.reshape(part_chunk, 2, n_blk, tile, total_inputs)
        doubled = jnp.concatenate([gram, gram], axis=-1)
        blocks = []
        for own in range(n_blk):
            start = (own - steps + 1) % n_blk * tile
            blocks.append(doubled[:, :, own, :, start : start + rows])
        return jnp.stack(blocks) * (1.0 / SPECTRA)

    def half_output(banded, half):
        returned = lax.all_to_all(banded, "blk", 0, 0, tiled=True)
        returned = returned.reshape(n_blk * part_chunk, 2 * tile * rows)
        source = np.arange(n_blk)[:, None] * chunk + half * part_chunk + np.arange(part_chunk)[None, :]
        select = (source.reshape(-1, 1) == np.arange(n_blk * chunk)[None, :]).astype(np.float32)
        return jnp.einsum("ax,ac->xc", returned, jnp.asarray(select), precision=lax.Precision.HIGHEST)

    spectra_parts = [half_spectra(half) for half in range(halves)]
    band_parts = [half_band(spectra) for spectra in spectra_parts]
    turned = half_output(band_parts[0], 0)
    for half in range(1, halves):
        turned = turned + half_output(band_parts[half], half)
    turned = turned.reshape(2, tile, steps, tile, n_blk * chunk)[:, :, ::-1]
    return turned.transpose(0, 2, 3, 1, 4)


def solution(mesh):
    placed = (P(("blk", "freq"), None), P(), P("blk"), P())
    return jax.shard_map(
        per_device,
        mesh=mesh,
        in_specs=placed,
        out_specs=P(None, None, None, "blk", "freq"),
        check_vma=False,
    )
```

```python
import math

import numpy as np
import jax
import jax.numpy as jnp
from jax import lax
from jax.sharding import PartitionSpec as P

TAPS = 4
SPECTRA = 256


def phase_table(chans, rows, period):
    sample_index = jnp.arange(rows, dtype=jnp.int32)
    product = sample_index[:, None] * chans[None, :] % period
    phase_arg = product.astype(jnp.float32) * (math.pi / (period // 2))
    return jnp.cos(phase_arg), jnp.sin(phase_arg)


def make_table(chans, channel_count):
    period = 2 * channel_count
    inner_rows = 64
    outer_rows = period // inner_rows
    inner_cos, inner_sin = phase_table(chans, inner_rows, period)
    outer_chans = chans * inner_rows % period
    outer_cos, outer_sin = phase_table(outer_chans, outer_rows, period)
    scale = 1.0 / math.sqrt(channel_count)
    cos = outer_cos[:, None, :] * inner_cos[None] - outer_sin[:, None, :] * inner_sin[None]
    sin = outer_sin[:, None, :] * inner_cos[None] + outer_cos[:, None, :] * inner_sin[None]
    columns = chans.shape[0]
    return (cos * scale).reshape(period, columns), (sin * -scale).reshape(period, columns)


def per_device(raw_voltages, filter_taps, input_order, chan_order):
    n_blk = lax.axis_size("blk")
    n_freq = lax.axis_size("freq")
    n_dev = n_blk * n_freq
    channel_count = chan_order.shape[0]
    width = channel_count // n_freq
    chunk = width // n_blk
    halves = 2
    part_chunk = chunk // halves
    steps = n_blk // 2 + 1
    tile = input_order.shape[0]
    local_inputs = raw_voltages.shape[0]
    total_inputs = n_dev * local_inputs
    frame = 2 * channel_count
    rows = steps * tile

    spread = jnp.broadcast_to(input_order.astype(jnp.float32)[None], (n_dev, tile))
    slot_order = lax.all_to_all(spread, ("blk", "freq"), 0, 0, tiled=True)
    slot_order = slot_order.reshape(n_blk, n_freq, tile)[:, 0].reshape(-1).astype(jnp.int32)

    frames = raw_voltages.astype(jnp.float32).reshape(local_inputs, SPECTRA + TAPS - 1, frame)
    filtered = filter_taps[0] * frames[:, 0:SPECTRA]
    for tap_index in range(1, TAPS):
        filtered = filtered + filter_taps[tap_index] * frames[:, tap_index : tap_index + SPECTRA]
    filtered = filtered.reshape(local_inputs * SPECTRA, frame)

    dest_b = np.arange(n_blk)[:, None, None]
    dest_f = np.arange(n_freq)[None, :, None]

    def half_spectra(half):
        within = np.arange(half * part_chunk, (half + 1) * part_chunk)[None, None, :]
        position = (dest_f * width + dest_b * chunk + within).reshape(-1)
        cos_table, sin_table = make_table(chan_order[position], channel_count)
        parts = [
            jnp.einsum("mc,nm->cn", part, filtered, precision=lax.Precision.HIGH)
            for part in (cos_table, sin_table)
        ]
        spectra = jnp.stack(parts, axis=1).astype(jnp.bfloat16)
        spectra = spectra.reshape(n_dev, part_chunk, 2, local_inputs, SPECTRA)
        return spectra.transpose(0, 1, 3, 2, 4)

    def half_band(spectra):
        gathered = lax.all_to_all(spectra, ("blk", "freq"), 0, 0, tiled=True)
        gathered = gathered.transpose(1, 0, 2, 3, 4).reshape(part_chunk, total_inputs, 2, SPECTRA)
        slotted = jnp.take(gathered, slot_order, axis=1)
        plain = slotted.reshape(part_chunk, total_inputs, 2 * SPECTRA)
        rotated = jnp.concatenate([slotted[:, :, 1], -slotted[:, :, 0]], axis=2)
        both = jnp.concatenate([plain, rotated], axis=1)
        gram = jnp.einsum("kat,kpt->kap", both, plain, preferred_element_type=jnp.float32)
        gram = gram.reshape(part_chunk, 2, n_blk, tile, total_inputs)
        doubled = jnp.concatenate([gram, gram], axis=-1)
        near, far = [], []
        for own in range(n_blk):
            far_start = (own - steps + 1) % n_blk * tile
            near_start = far_start + tile
            near.append(doubled[:, :, own, :, near_start : near_start + rows - tile])
            far.append(doubled[:, :, own, :, far_start : far_start + tile])
        near = jnp.stack(near) * (1.0 / SPECTRA)
        far = jnp.stack(far).reshape(n_blk, part_chunk * 2, tile * tile) * (1.0 / SPECTRA)
        return near, far

    def half_output(band, half):
        near, far = band
        source = np.arange(n_blk)[:, None] * chunk + half * part_chunk + np.arange(part_chunk)[None, :]
        select = (source[:, :, None] == np.arange(n_blk * chunk)[None, None, :]).astype(np.float32)
        select = jnp.asarray(select)
        near = lax.all_to_all(near, "blk", 0, 0, tiled=True)
        near = near.reshape(n_blk, part_chunk, -1)
        near = jnp.einsum("bkx,bkc->xc", near, select, precision=lax.Precision.HIGHEST)
        near = near.reshape(2, tile, steps - 1, tile, n_blk * chunk)[:, :, ::-1]
        far = lax.all_to_all(far, "blk", 0, 0, tiled=True)
        far = far.reshape(n_blk, part_chunk, 2, tile * tile)
        far = jnp.einsum("bkrx,bkc->rxc", far, select, precision=lax.Precision.HIGHEST)
        far = far.reshape(2, tile, 1, tile, n_blk * chunk)
        return jnp.concatenate([near, far], axis=2)

    spectra_parts = [half_spectra(half) for half in range(halves)]
    band_parts = [half_band(spectra) for spectra in spectra_parts]
    turned = half_output(band_parts[0], 0)
    for half in range(1, halves):
        turned = turned + half_output(band_parts[half], half)
    return turned.transpose(0, 2, 3, 1, 4)


def solution(mesh):
    placed = (P(("blk", "freq"), None), P(), P("blk"), P())
    return jax.shard_map(
        per_device,
        mesh=mesh,
        in_specs=placed,
        out_specs=P(None, None, None, "blk", "freq"),
        check_vma=False,
    )
```

```python
import math

import numpy as np
import jax
import jax.numpy as jnp
from jax import lax
from jax.sharding import PartitionSpec as P

TAPS = 4
SPECTRA = 256


def phase_table(chans, rows, period):
    sample_index = jnp.arange(rows, dtype=jnp.int32)
    product = sample_index[:, None] * chans[None, :] % period
    phase_arg = product.astype(jnp.float32) * (math.pi / (period // 2))
    return jnp.cos(phase_arg), jnp.sin(phase_arg)


def make_table(chans, channel_count):
    period = 2 * channel_count
    inner_rows = 64
    outer_rows = period // inner_rows
    inner_cos, inner_sin = phase_table(chans, inner_rows, period)
    outer_chans = chans * inner_rows % period
    outer_cos, outer_sin = phase_table(outer_chans, outer_rows, period)
    scale = 1.0 / math.sqrt(channel_count)
    cos = outer_cos[:, None, :] * inner_cos[None] - outer_sin[:, None, :] * inner_sin[None]
    sin = outer_sin[:, None, :] * inner_cos[None] + outer_cos[:, None, :] * inner_sin[None]
    columns = chans.shape[0]
    return (cos * scale).reshape(period, columns), (sin * -scale).reshape(period, columns)


def per_device(raw_voltages, filter_taps, input_order, chan_order):
    n_blk = lax.axis_size("blk")
    n_freq = lax.axis_size("freq")
    n_dev = n_blk * n_freq
    channel_count = chan_order.shape[0]
    width = channel_count // n_freq
    chunk = width // n_blk
    halves = 2
    part_chunk = chunk // halves
    steps = n_blk // 2 + 1
    tile = input_order.shape[0]
    local_inputs = raw_voltages.shape[0]
    total_inputs = n_dev * local_inputs
    frame = 2 * channel_count
    rows = steps * tile
    reverse_tiles = (
        (n_blk - 1 - np.arange(n_blk))[:, None] * tile + np.arange(tile)[None, :]
    ).reshape(-1)

    spread = jnp.broadcast_to(input_order.astype(jnp.float32)[None], (n_dev, tile))
    slot_order = lax.all_to_all(spread, ("blk", "freq"), 0, 0, tiled=True)
    slot_order = slot_order.reshape(n_blk, n_freq, tile)[:, 0].reshape(-1).astype(jnp.int32)

    frames = raw_voltages.astype(jnp.float32).reshape(local_inputs, SPECTRA + TAPS - 1, frame)
    filtered = filter_taps[0] * frames[:, 0:SPECTRA]
    for tap_index in range(1, TAPS):
        filtered = filtered + filter_taps[tap_index] * frames[:, tap_index : tap_index + SPECTRA]
    filtered = filtered.reshape(local_inputs * SPECTRA, frame)

    dest_b = np.arange(n_blk)[:, None, None]
    dest_f = np.arange(n_freq)[None, :, None]

    def half_spectra(half):
        within = np.arange(half * part_chunk, (half + 1) * part_chunk)[None, None, :]
        position = (dest_f * width + dest_b * chunk + within).reshape(-1)
        cos_table, sin_table = make_table(chan_order[position], channel_count)
        parts = [
            jnp.einsum("mc,nm->cn", part, filtered, precision=lax.Precision.HIGH)
            for part in (cos_table, sin_table)
        ]
        spectra = jnp.stack(parts, axis=1).astype(jnp.bfloat16)
        spectra = spectra.reshape(n_dev, part_chunk, 2, local_inputs, SPECTRA)
        return spectra.transpose(0, 1, 3, 2, 4)

    def half_band(spectra):
        gathered = lax.all_to_all(spectra, ("blk", "freq"), 0, 0, tiled=True)
        gathered = gathered.transpose(1, 0, 2, 3, 4).reshape(part_chunk, total_inputs, 2, SPECTRA)
        slotted = jnp.take(gathered, slot_order, axis=1)
        plain = slotted.reshape(part_chunk, total_inputs, 2 * SPECTRA)
        rotated = jnp.concatenate([slotted[:, :, 1], -slotted[:, :, 0]], axis=2)
        both = jnp.concatenate([plain, rotated], axis=1)
        partners = jnp.take(gathered, slot_order[reverse_tiles], axis=1)
        partners = partners.reshape(part_chunk, total_inputs, 2 * SPECTRA)
        gram = jnp.einsum("kat,kpt->kap", both, partners, preferred_element_type=jnp.float32)
        gram = gram.reshape(part_chunk, 2, n_blk, tile, total_inputs)
        doubled = jnp.concatenate([gram, gram], axis=-1)
        near, far = [], []
        for own in range(n_blk):
            near_start = (n_blk - 1 - own) * tile
            far_start = near_start + rows - tile
            near.append(doubled[:, :, own, :, near_start:far_start])
            far.append(doubled[:, :, own, :, far_start : far_start + tile])
        near = jnp.stack(near) * (1.0 / SPECTRA)
        far = jnp.stack(far).reshape(n_blk, part_chunk * 2, tile * tile) * (1.0 / SPECTRA)
        return near, far

    def half_output(band, half):
        near, far = band
        source = np.arange(n_blk)[:, None] * chunk + half * part_chunk + np.arange(part_chunk)[None, :]
        select = (source[:, :, None] == np.arange(n_blk * chunk)[None, None, :]).astype(np.float32)
        select = jnp.asarray(select)
        near = lax.all_to_all(near, "blk", 0, 0, tiled=True)
        near = near.reshape(n_blk, part_chunk, -1)
        near = jnp.einsum("bkx,bkc->xc", near, select, precision=lax.Precision.HIGHEST)
        near = near.reshape(2, tile, steps - 1, tile, n_blk * chunk)
        far = lax.all_to_all(far, "blk", 0, 0, tiled=True)
        far = far.reshape(n_blk, part_chunk, 2, tile * tile)
        far = jnp.einsum("bkrx,bkc->rxc", far, select, precision=lax.Precision.HIGHEST)
        return near, far.reshape(2, tile, 1, tile, n_blk * chunk)

    spectra_parts = [half_spectra(half) for half in range(halves)]
    band_parts = [half_band(spectra) for spectra in spectra_parts]
    near, far = half_output(band_parts[0], 0)
    for half in range(1, halves):
        more_near, more_far = half_output(band_parts[half], half)
        near = near + more_near
        far = far + more_far
    return jnp.concatenate([near, far], axis=2).transpose(0, 2, 3, 1, 4)


def solution(mesh):
    placed = (P(("blk", "freq"), None), P(), P("blk"), P())
    return jax.shard_map(
        per_device,
        mesh=mesh,
        in_specs=placed,
        out_specs=P(None, None, None, "blk", "freq"),
        check_vma=False,
    )
```

```python
import math

import numpy as np
import jax
import jax.numpy as jnp
from jax import lax
from jax.sharding import PartitionSpec as P

TAPS = 4
SPECTRA = 256


def phase_table(chans, rows, period):
    sample_index = jnp.arange(rows, dtype=jnp.int32)
    product = chans[:, None] * sample_index[None, :] % period
    phase_arg = product.astype(jnp.float32) * (math.pi / (period // 2))
    return jnp.cos(phase_arg), jnp.sin(phase_arg)


def make_table(chans, channel_count):
    period = 2 * channel_count
    inner_rows = 64
    outer_rows = period // inner_rows
    inner_cos, inner_sin = phase_table(chans, inner_rows, period)
    outer_chans = chans * inner_rows % period
    outer_cos, outer_sin = phase_table(outer_chans, outer_rows, period)
    scale = 1.0 / math.sqrt(channel_count)
    cos = outer_cos[:, :, None] * inner_cos[:, None, :] - outer_sin[:, :, None] * inner_sin[:, None, :]
    sin = outer_sin[:, :, None] * inner_cos[:, None, :] + outer_cos[:, :, None] * inner_sin[:, None, :]
    columns = chans.shape[0]
    return (cos * scale).reshape(columns, period), (sin * -scale).reshape(columns, period)


def per_device(raw_voltages, filter_taps, input_order, chan_order):
    n_blk = lax.axis_size("blk")
    n_freq = lax.axis_size("freq")
    n_dev = n_blk * n_freq
    channel_count = chan_order.shape[0]
    width = channel_count // n_freq
    chunk = width // n_blk
    halves = 2
    part_chunk = chunk // halves
    steps = n_blk // 2 + 1
    tile = input_order.shape[0]
    local_inputs = raw_voltages.shape[0]
    total_inputs = n_dev * local_inputs
    frame = 2 * channel_count
    rows = steps * tile

    spread = jnp.broadcast_to(input_order.astype(jnp.float32)[None], (n_dev, tile))
    slot_order = lax.all_to_all(spread, ("blk", "freq"), 0, 0, tiled=True)
    slot_order = slot_order.reshape(n_blk, n_freq, tile)[:, 0].reshape(-1).astype(jnp.int32)

    frames = raw_voltages.astype(jnp.float32).reshape(local_inputs, SPECTRA + TAPS - 1, frame)
    filtered = filter_taps[0] * frames[:, 0:SPECTRA]
    for tap_index in range(1, TAPS):
        filtered = filtered + filter_taps[tap_index] * frames[:, tap_index : tap_index + SPECTRA]
    filtered = filtered.reshape(local_inputs * SPECTRA, frame)

    dest_b = np.arange(n_blk)[:, None, None]
    dest_f = np.arange(n_freq)[None, :, None]

    def half_spectra(half):
        within = np.arange(half * part_chunk, (half + 1) * part_chunk)[None, None, :]
        position = (dest_f * width + dest_b * chunk + within).reshape(-1)
        cos_table, sin_table = make_table(chan_order[position], channel_count)
        parts = [
            jnp.einsum("cm,nm->cn", part, filtered, precision=lax.Precision.HIGH)
            for part in (cos_table, sin_table)
        ]
        spectra = jnp.stack(parts, axis=1).astype(jnp.bfloat16)
        spectra = spectra.reshape(n_dev, part_chunk, 2, local_inputs, SPECTRA)
        return spectra.transpose(0, 1, 3, 2, 4)

    def half_band(spectra):
        gathered = lax.all_to_all(spectra, ("blk", "freq"), 0, 0, tiled=True)
        gathered = gathered.transpose(1, 0, 2, 3, 4).reshape(part_chunk, total_inputs, 2, SPECTRA)
        slotted = jnp.take(gathered, slot_order, axis=1)
        plain = slotted.reshape(part_chunk, total_inputs, 2 * SPECTRA)
        rotated = jnp.concatenate([slotted[:, :, 1], -slotted[:, :, 0]], axis=2)
        both = jnp.concatenate([plain, rotated], axis=1)
        gram = jnp.einsum("kat,kpt->kap", both, plain, preferred_element_type=jnp.float32)
        gram = gram.reshape(part_chunk, 2, n_blk, tile, total_inputs)
        doubled = jnp.concatenate([gram, gram], axis=-1)
        blocks = []
        for own in range(n_blk):
            start = (own - steps + 1) % n_blk * tile
            blocks.append(doubled[:, :, own, :, start : start + rows])
        return jnp.stack(blocks) * (1.0 / SPECTRA)

    def half_output(banded, half):
        returned = lax.all_to_all(banded, "blk", 0, 0, tiled=True)
        returned = returned.reshape(n_blk * part_chunk, 2 * tile * rows)
        source = np.arange(n_blk)[:, None] * chunk + half * part_chunk + np.arange(part_chunk)[None, :]
        select = (source.reshape(-1, 1) == np.arange(n_blk * chunk)[None, :]).astype(np.float32)
        return jnp.einsum("ax,ac->xc", returned, jnp.asarray(select), precision=lax.Precision.HIGHEST)

    spectra_parts = [half_spectra(half) for half in range(halves)]
    band_parts = [half_band(spectra) for spectra in spectra_parts]
    turned = half_output(band_parts[0], 0)
    for half in range(1, halves):
        turned = turned + half_output(band_parts[half], half)
    turned = turned.reshape(2, tile, steps, tile, n_blk * chunk)[:, :, ::-1]
    return turned.transpose(0, 2, 3, 1, 4)


def solution(mesh):
    placed = (P(("blk", "freq"), None), P(), P("blk"), P())
    return jax.shard_map(
        per_device,
        mesh=mesh,
        in_specs=placed,
        out_specs=P(None, None, None, "blk", "freq"),
        check_vma=False,
    )
```

```python
import math

import numpy as np
import jax
import jax.numpy as jnp
from jax import lax
from jax.sharding import PartitionSpec as P


TAPS = 4
SPECTRA = 256


def phase_table(chans, rows, period):
    sample_index = jnp.arange(rows, dtype=jnp.int32)
    product = sample_index[:, None] * chans[None, :] % period
    phase_arg = product.astype(jnp.float32) * (math.pi / (period // 2))
    return jnp.cos(phase_arg), jnp.sin(phase_arg)


def make_table(chans, channel_count):
    period = 2 * channel_count
    inner_rows = 64
    outer_rows = period // inner_rows
    inner_cos, inner_sin = phase_table(chans, inner_rows, period)
    outer_chans = chans * inner_rows % period
    outer_cos, outer_sin = phase_table(outer_chans, outer_rows, period)
    scale = 1.0 / math.sqrt(channel_count)
    cos = outer_cos[:, None, :] * inner_cos[None] - outer_sin[:, None, :] * inner_sin[None]
    sin = outer_sin[:, None, :] * inner_cos[None] + outer_cos[:, None, :] * inner_sin[None]
    columns = chans.shape[0]
    return (cos * scale).reshape(period, columns), (sin * -scale).reshape(period, columns)


def per_device(raw_voltages, filter_taps, input_order, chan_order):
    n_blk = lax.axis_size("blk")
    n_freq = lax.axis_size("freq")
    n_dev = n_blk * n_freq
    channel_count = chan_order.shape[0]
    width = channel_count // n_freq
    chunk = width // n_blk
    halves = 2
    part_chunk = chunk // halves
    steps = n_blk // 2 + 1
    tile = input_order.shape[0]
    local_inputs = raw_voltages.shape[0]
    total_inputs = n_dev * local_inputs
    frame = 2 * channel_count
    rows = steps * tile
    reverse_tiles = (
        (n_blk - 1 - np.arange(n_blk))[:, None] * tile + np.arange(tile)[None, :]
    ).reshape(-1)

    spread = jnp.broadcast_to(input_order.astype(jnp.float32)[None], (n_dev, tile))
    slot_order = lax.all_to_all(spread, ("blk", "freq"), 0, 0, tiled=True)
    slot_order = slot_order.reshape(n_blk, n_freq, tile)[:, 0].reshape(-1).astype(jnp.int32)

    frames = raw_voltages.astype(jnp.float32).reshape(local_inputs, SPECTRA + TAPS - 1, frame)
    filtered = filter_taps[0] * frames[:, 0:SPECTRA]
    for tap_index in range(1, TAPS):
        filtered = filtered + filter_taps[tap_index] * frames[:, tap_index : tap_index + SPECTRA]
    filtered = filtered.reshape(local_inputs * SPECTRA, frame)

    dest_b = np.arange(n_blk)[:, None, None]
    dest_f = np.arange(n_freq)[None, :, None]

    def half_spectra(half):
        within = np.arange(half * part_chunk, (half + 1) * part_chunk)[None, None, :]
        position = (dest_f * width + dest_b * chunk + within).reshape(-1)
        cos_table, sin_table = make_table(chan_order[position], channel_count)
        parts = [
            jnp.einsum("mc,nm->cn", part, filtered, precision=lax.Precision.HIGH)
            for part in (cos_table, sin_table)
        ]
        spectra = jnp.stack(parts, axis=1).astype(jnp.bfloat16)
        spectra = spectra.reshape(n_dev, part_chunk, 2, local_inputs, SPECTRA)
        return spectra.transpose(0, 1, 3, 2, 4)

    def half_band(spectra, earlier):
        gathered = lax.all_to_all(spectra, ("blk", "freq"), 0, 0, tiled=True)
        if earlier is not None:
            earlier, gathered = lax.optimization_barrier((earlier, gathered))
        gathered = gathered.transpose(1, 0, 2, 3, 4).reshape(part_chunk, total_inputs, 2, SPECTRA)
        slotted = jnp.take(gathered, slot_order, axis=1)
        plain = slotted.reshape(part_chunk, total_inputs, 2 * SPECTRA)
        rotated = jnp.concatenate([slotted[:, :, 1], -slotted[:, :, 0]], axis=2)
        both = jnp.concatenate([plain, rotated], axis=1)
        partners = jnp.take(gathered, slot_order[reverse_tiles], axis=1)
        partners = partners.reshape(part_chunk, total_inputs, 2 * SPECTRA)
        gram = jnp.einsum("kat,kpt->kap", both, partners, preferred_element_type=jnp.float32)
        gram = gram.reshape(part_chunk, 2, n_blk, tile, total_inputs)
        doubled = jnp.concatenate([gram, gram], axis=-1)
        blocks = []
        for own in range(n_blk):
            start = (n_blk - 1 - own) * tile
            blocks.append(doubled[:, :, own, :, start : start + rows])
        return jnp.stack(blocks) * (1.0 / SPECTRA)

    def half_output(banded, half):
        returned = lax.all_to_all(banded, "blk", 0, 0, tiled=True)
        returned = returned.reshape(n_blk * part_chunk, 2 * tile * rows)
        source = np.arange(n_blk)[:, None] * chunk + half * part_chunk + np.arange(part_chunk)[None, :]
        select = (source.reshape(-1, 1) == np.arange(n_blk * chunk)[None, :]).astype(np.float32)
        return jnp.einsum("ax,ac->xc", returned, jnp.asarray(select), precision=lax.Precision.HIGHEST)

    spectra_parts = [half_spectra(half) for half in range(halves)]
    band_parts = []
    for spectra in spectra_parts:
        band_parts.append(half_band(spectra, band_parts[-1] if band_parts else None))
    turned = half_output(band_parts[0], 0)
    for half in range(1, halves):
        turned = turned + half_output(band_parts[half], half)
    turned = turned.reshape(2, tile, steps, tile, n_blk * chunk)
    return turned.transpose(0, 2, 3, 1, 4)


def solution(mesh):
    placed = (P(("blk", "freq"), None), P(), P("blk"), P())
    return jax.shard_map(
        per_device,
        mesh=mesh,
        in_specs=placed,
        out_specs=P(None, None, None, "blk", "freq"),
        check_vma=False,
    )
```

```python
import math

import numpy as np
import jax
import jax.numpy as jnp
from jax import lax
from jax.sharding import PartitionSpec as P


TAPS = 4
SPECTRA = 256


def phase_table(chans, rows, period):
    sample_index = jnp.arange(rows, dtype=jnp.int32)
    product = sample_index[:, None] * chans[None, :] % period
    phase_arg = product.astype(jnp.float32) * (math.pi / (period // 2))
    return jnp.cos(phase_arg), jnp.sin(phase_arg)


def make_table(chans, channel_count):
    period = 2 * channel_count
    inner_rows = 64
    outer_rows = period // inner_rows
    inner_cos, inner_sin = phase_table(chans, inner_rows, period)
    outer_chans = chans * inner_rows % period
    outer_cos, outer_sin = phase_table(outer_chans, outer_rows, period)
    scale = 1.0 / math.sqrt(channel_count)
    cos = outer_cos[:, None, :] * inner_cos[None] - outer_sin[:, None, :] * inner_sin[None]
    sin = outer_sin[:, None, :] * inner_cos[None] + outer_cos[:, None, :] * inner_sin[None]
    columns = chans.shape[0]
    return (cos * scale).reshape(period, columns), (sin * -scale).reshape(period, columns)


def per_device(raw_voltages, filter_taps, input_order, chan_order):
    n_blk = lax.axis_size("blk")
    n_freq = lax.axis_size("freq")
    n_dev = n_blk * n_freq
    channel_count = chan_order.shape[0]
    width = channel_count // n_freq
    chunk = width // n_blk
    halves = 2
    part_chunk = chunk // halves
    steps = n_blk // 2 + 1
    tile = input_order.shape[0]
    local_inputs = raw_voltages.shape[0]
    total_inputs = n_dev * local_inputs
    frame = 2 * channel_count
    rows = steps * tile

    spread = jnp.broadcast_to(input_order.astype(jnp.float32)[None], (n_dev, tile))
    slot_order = lax.all_to_all(spread, ("blk", "freq"), 0, 0, tiled=True)
    slot_order = slot_order.reshape(n_blk, n_freq, tile)[:, 0].reshape(-1).astype(jnp.int32)

    frames = raw_voltages.astype(jnp.float32).reshape(local_inputs, SPECTRA + TAPS - 1, frame)
    filtered = filter_taps[0] * frames[:, 0:SPECTRA]
    for tap_index in range(1, TAPS):
        filtered = filtered + filter_taps[tap_index] * frames[:, tap_index : tap_index + SPECTRA]
    filtered = filtered.reshape(local_inputs * SPECTRA, frame)

    dest_b = np.arange(n_blk)[:, None, None]
    dest_f = np.arange(n_freq)[None, :, None]

    def half_spectra(half):
        within = np.arange(half * part_chunk, (half + 1) * part_chunk)[None, None, :]
        position = (dest_f * width + dest_b * chunk + within).reshape(-1)
        cos_table, sin_table = make_table(chan_order[position], channel_count)
        parts = [
            jnp.einsum("mc,nm->cn", part, filtered, precision=lax.Precision.HIGH)
            for part in (cos_table, sin_table)
        ]
        spectra = jnp.stack(parts, axis=1).astype(jnp.bfloat16)
        spectra = spectra.reshape(n_dev, part_chunk, 2, local_inputs, SPECTRA)
        return spectra.transpose(0, 1, 3, 2, 4)

    def half_band(spectra, earlier):
        gathered = lax.all_to_all(spectra, ("blk", "freq"), 0, 0, tiled=True)
        if earlier is not None:
            earlier, gathered = lax.optimization_barrier((earlier, gathered))
        gathered = gathered.transpose(1, 0, 2, 3, 4).reshape(part_chunk, total_inputs, 2, SPECTRA)
        slotted = jnp.take(gathered, slot_order, axis=1)
        plain = slotted.reshape(part_chunk, total_inputs, 2 * SPECTRA)
        rotated = jnp.concatenate([slotted[:, :, 1], -slotted[:, :, 0]], axis=2)
        both = jnp.concatenate([plain, rotated], axis=1)
        gram = jnp.einsum("kat,kpt->kap", both, plain, preferred_element_type=jnp.float32)
        gram = gram.reshape(part_chunk, 2, n_blk, tile, total_inputs)
        doubled = jnp.concatenate([gram, gram], axis=-1)
        blocks = []
        for own in range(n_blk):
            start = (own - steps + 1) % n_blk * tile
            blocks.append(doubled[:, :, own, :, start : start + rows])
        return jnp.stack(blocks) * (1.0 / SPECTRA)

    def half_output(banded, half):
        returned = lax.all_to_all(banded, "blk", 0, 0, tiled=True)
        returned = returned.reshape(n_blk * part_chunk, 2 * tile * rows)
        source = np.arange(n_blk)[:, None] * chunk + half * part_chunk + np.arange(part_chunk)[None, :]
        select = (source.reshape(-1, 1) == np.arange(n_blk * chunk)[None, :]).astype(np.float32)
        high = returned.astype(jnp.bfloat16)
        rest = returned - high.astype(jnp.float32)
        middle = rest.astype(jnp.bfloat16)
        low = (rest - middle.astype(jnp.float32)).astype(jnp.bfloat16)
        pieces = jnp.concatenate([high, middle, low], axis=0)
        select = jnp.asarray(np.concatenate([select] * 3, axis=0), dtype=jnp.bfloat16)
        return jnp.einsum("ax,ac->xc", pieces, select, preferred_element_type=jnp.float32)

    spectra_parts = [half_spectra(half) for half in range(halves)]
    band_parts = []
    for spectra in spectra_parts:
        band_parts.append(half_band(spectra, band_parts[-1] if band_parts else None))
    turned = half_output(band_parts[0], 0)
    for half in range(1, halves):
        turned = turned + half_output(band_parts[half], half)
    turned = turned.reshape(2, tile, steps, tile, n_blk * chunk)[:, :, ::-1]
    return turned.transpose(0, 2, 3, 1, 4)


def solution(mesh):
    placed = (P(("blk", "freq"), None), P(), P("blk"), P())
    return jax.shard_map(
        per_device,
        mesh=mesh,
        in_specs=placed,
        out_specs=P(None, None, None, "blk", "freq"),
        check_vma=False,
    )
```

```python
import math

import numpy as np
import jax
import jax.numpy as jnp
from jax import lax
from jax.sharding import PartitionSpec as P


TAPS = 4
SPECTRA = 256


def phase_table(chans, rows, period):
    sample_index = jnp.arange(rows, dtype=jnp.int32)
    product = sample_index[:, None] * chans[None, :] % period
    phase_arg = product.astype(jnp.float32) * (math.pi / (period // 2))
    return jnp.cos(phase_arg), jnp.sin(phase_arg)


def make_table(chans, channel_count):
    period = 2 * channel_count
    inner_rows = 64
    outer_rows = period // inner_rows
    inner_cos, inner_sin = phase_table(chans, inner_rows, period)
    outer_chans = chans * inner_rows % period
    outer_cos, outer_sin = phase_table(outer_chans, outer_rows, period)
    scale = 1.0 / math.sqrt(channel_count)
    cos = outer_cos[:, None, :] * inner_cos[None] - outer_sin[:, None, :] * inner_sin[None]
    sin = outer_sin[:, None, :] * inner_cos[None] + outer_cos[:, None, :] * inner_sin[None]
    columns = chans.shape[0]
    return (cos * scale).reshape(period, columns), (sin * -scale).reshape(period, columns)


def per_device(raw_voltages, filter_taps, input_order, chan_order):
    n_blk = lax.axis_size("blk")
    n_freq = lax.axis_size("freq")
    n_dev = n_blk * n_freq
    channel_count = chan_order.shape[0]
    width = channel_count // n_freq
    chunk = width // n_blk
    halves = 2
    part_chunk = chunk // halves
    steps = n_blk // 2 + 1
    tile = input_order.shape[0]
    local_inputs = raw_voltages.shape[0]
    total_inputs = n_dev * local_inputs
    frame = 2 * channel_count
    rows = steps * tile

    spread = jnp.broadcast_to(input_order.astype(jnp.float32)[None], (n_dev, tile))
    slot_order = lax.all_to_all(spread, ("blk", "freq"), 0, 0, tiled=True)
    slot_order = slot_order.reshape(n_blk, n_freq, tile)[:, 0].reshape(-1).astype(jnp.int32)

    frames = raw_voltages.astype(jnp.float32).reshape(local_inputs, SPECTRA + TAPS - 1, frame)
    filtered = filter_taps[0] * frames[:, 0:SPECTRA]
    for tap_index in range(1, TAPS):
        filtered = filtered + filter_taps[tap_index] * frames[:, tap_index : tap_index + SPECTRA]
    filtered = filtered.reshape(local_inputs * SPECTRA, frame)

    dest_b = np.arange(n_blk)[:, None, None]
    dest_f = np.arange(n_freq)[None, :, None]

    def half_spectra(half):
        within = np.arange(half * part_chunk, (half + 1) * part_chunk)[None, None, :]
        position = (dest_f * width + dest_b * chunk + within).reshape(-1)
        cos_table, sin_table = make_table(chan_order[position], channel_count)
        parts = [
            jnp.einsum("mc,nm->cn", part, filtered, precision=lax.Precision.HIGH)
            for part in (cos_table, sin_table)
        ]
        spectra = jnp.stack(parts, axis=1).astype(jnp.bfloat16)
        spectra = spectra.reshape(n_dev, part_chunk, 2, local_inputs, SPECTRA)
        return spectra.transpose(0, 1, 3, 2, 4)

    def half_band(spectra, earlier):
        gathered = lax.all_to_all(spectra, ("blk", "freq"), 0, 0, tiled=True)
        if earlier is not None:
            earlier, gathered = lax.optimization_barrier((earlier, gathered))
        gathered = gathered.transpose(1, 0, 2, 3, 4).reshape(part_chunk, total_inputs, 2, SPECTRA)
        slotted = jnp.take(gathered, slot_order, axis=1)
        plain = slotted.reshape(part_chunk, total_inputs, 2 * SPECTRA)
        rotated = jnp.concatenate([slotted[:, :, 1], -slotted[:, :, 0]], axis=2)
        both = jnp.concatenate([plain, rotated], axis=1)
        gram = jnp.einsum("kat,kpt->kap", both, plain, preferred_element_type=jnp.float32)
        gram = gram.reshape(part_chunk, 2, n_blk, tile, total_inputs)
        doubled = jnp.concatenate([gram, gram], axis=-1)
        blocks = []
        for own in range(n_blk):
            start = (own - steps + 1) % n_blk * tile
            blocks.append(doubled[:, :, own, :, start : start + rows])
        return jnp.stack(blocks)

    def half_output(banded, half):
        returned = lax.all_to_all(banded, "blk", 0, 0, tiled=True)
        returned = returned.reshape(n_blk * part_chunk, 2 * tile * rows)
        source = np.arange(n_blk)[:, None] * chunk + half * part_chunk + np.arange(part_chunk)[None, :]
        select = (source.reshape(-1, 1) == np.arange(n_blk * chunk)[None, :]).astype(np.float32)
        select = select * (1.0 / SPECTRA)
        return jnp.einsum("ax,ac->xc", returned, jnp.asarray(select), precision=lax.Precision.HIGHEST)

    spectra_parts = [half_spectra(half) for half in range(halves)]
    band_parts = []
    for spectra in spectra_parts:
        band_parts.append(half_band(spectra, band_parts[-1] if band_parts else None))
    turned = half_output(band_parts[0], 0)
    for half in range(1, halves):
        turned = turned + half_output(band_parts[half], half)
    turned = turned.reshape(2, tile, steps, tile, n_blk * chunk)[:, :, ::-1]
    return turned.transpose(0, 2, 3, 1, 4)


def solution(mesh):
    placed = (P(("blk", "freq"), None), P(), P("blk"), P())
    return jax.shard_map(
        per_device,
        mesh=mesh,
        in_specs=placed,
        out_specs=P(None, None, None, "blk", "freq"),
        check_vma=False,
    )
```
